256 devices in a mesh: dp: 8 (over x, core), expert: 32 (over y, z).
Axes of the slice: x: 4, y: 4, z: 8, core: 2. Of those that a mesh axis runs over, the one named last changes fastest.
Arguments:
- tokens: bfloat16 [32768, 2048], P(('dp', 'expert')), may hold values from -6 to 6
- router_weight: bfloat16 [2048, 64], replicated, may hold values from -0.125 to 0.125
- expert_ids: int32 [32768, 8], P(('dp', 'expert')), may hold values from 0 to 63, all different within a row; in each aligned block of 128 rows (0 to 127, 128 to 255, ...) at most 24 rows name the same one
- gate_matrix: bfloat16 [2048, 64, 384], P('dp', 'expert'), may hold values from -0.125 to 0.125
- up_matrix: bfloat16 [2048, 64, 384], P('dp', 'expert'), may hold values from -0.125 to 0.125
- down_matrix: bfloat16 [2048, 64, 384], P('dp', 'expert'), may hold values from -0.3125 to 0.3125
- cotangent: bfloat16 [32768, 2048], P(('dp', 'expert')), may hold values from -3 to 3
Outputs:
- mixed_out: bfloat16 [32768, 2048], P(('dp', 'expert'))
- token_grad: bfloat16 [32768, 2048], P(('dp', 'expert'))
- gate_grad: bfloat16 [2048, 64, 384], P('dp', 'expert')
- up_grad: bfloat16 [2048, 64, 384], P('dp', 'expert')
- down_grad: bfloat16 [2048, 64, 384], P('dp', 'expert')
- router_grad: float32 [2048, 64], replicated
The draws below stay inside these ranges and needn't reach their ends.
Inputs may be any that keep to these rules, and one draw needn't show every extreme that they name: `expert_ids`: each row names 8 different experts and every expert is named by some row. Among the rows of one device no expert is named more than 24 times, and in some device's rows some expert is named exactly 24 times.
All inputs are finite; a program needn't handle non-finite values.
Results may differ from the reference program's by a relative error of at most 0.014.
Values may be sent and summed in bfloat16 or wider, within the bound.
No kernel may reach another device: no remote copies, remote signals or barrier semaphores. Data moves between devices by JAX's collectives and lax.ppermute only.
A program may use at most 128 MiB of HBM per device.

```python
import math
import jax
import jax.numpy as jnp
import numpy as np
from jax import lax

D = 2048
FF = 384
TOP = 8
TOK_DEV = 128
EXPERTS = 64
CAP = 24
TOKENS = 32768
N_DP = 8
N_EXPERT = 32


def steps_of(stream_key, dims, shards, smallest, top_value):
    def one(dim, shards_of):
        steps = jax.random.uniform(jax.random.fold_in(jax.random.fold_in(stream_key, 6), dim), (shards_of,), jnp.float32, smallest / len(shards), top_value / len(shards))
        return jnp.repeat(jnp.exp(steps), dims[dim] // shards_of).reshape((-1,) + (1,) * (len(dims) - dim - 1))

    loudness = one(*shards[0])
    for cut in shards[1:]:
        loudness = loudness * one(*cut)
    return loudness


def assign_block(own_key, own, number, rows, amount, top, bound, skew):
    ranking = jax.random.permutation(own_key, amount)
    crowded, usual = portions_of(amount, rows * top, bound, skew, True), portions_of(amount, rows * top, bound, skew, False)
    places = jnp.arange(amount)

    def named(tallies, offset_by):
        used = int((tallies > 0).sum())
        fixed = max(1, used // 4)
        shifted = fixed + (places - fixed + offset_by * (used - fixed)) % max(1, amount - fixed)
        return jnp.zeros((amount,), jnp.int32).at[ranking[jnp.where(places < fixed, places, shifted)]].set(jnp.asarray(tallies, jnp.int32))

    tallies = jnp.where(number % 4 == 0, named(crowded, number // 4), named(usual, number - number // 4 - 1))
    mixed = jax.random.permutation(jax.random.fold_in(own, 3), amount)
    donor, sink = mixed[0:amount // 2 * 2:2], mixed[1:amount // 2 * 2:2]
    room = jnp.minimum(tallies[donor] - 1, bound - tallies[sink]) // 2
    room = jnp.where((donor == ranking[0]) | (sink == ranking[0]) | (tallies[sink] == 0), 0, jnp.maximum(room, 0))
    shifted = jax.random.randint(jax.random.fold_in(own, 4), (amount // 2,), 0, 1 << 20) % (room + 1)
    tallies = tallies.at[donor].add(-shifted).at[sink].add(shifted)
    labels = jnp.searchsorted(jnp.cumsum(tallies), jnp.arange(rows * top), side="right").astype(jnp.int32)
    grid = labels.reshape(top, rows).T
    grid = grid[jax.random.permutation(jax.random.fold_in(own, 1), rows)]
    offset_by = jax.random.randint(jax.random.fold_in(own, 2), (rows, 1), 0, top)
    return jnp.take_along_axis(grid, (jnp.arange(top)[None, :] + offset_by) % top, axis=1)


def portions_of(number_of, total, most, slope, full):
    portions = [(1 << 20) // math.isqrt(standing ** slope) + 1 for standing in range(1, number_of + 1)]
    largest = most if full else min(most, max(-(-total // number_of), total * portions[0] // sum(portions)))
    least = 1 if total - largest >= number_of - 1 else 0
    holding, spare = [largest] + [least] * (number_of - 1), total - largest - least * (number_of - 1)
    while spare > 0:
        free = [i for i in range(1, number_of) if holding[i] < largest] or [i for i in range(1, number_of) if holding[i] < most]
        mass, remaining = sum([portions[i] for i in free]), spare
        for i in free:
            extra = min(most - holding[i], max(1, remaining * portions[i] // mass), spare)
            holding[i] = holding[i] + extra
            spare = spare - extra
    return np.array(holding)


def noise(stream_key, dims, spread, reach, pieces=(), held_as=jnp.bfloat16):
    loudness = steps_of(stream_key, dims, pieces, -0.22, 0.18) if pieces else 1.0
    values = jax.random.normal(stream_key, dims, jnp.float32) * spread * loudness
    return jnp.minimum(jnp.maximum(values, -reach), reach).astype(held_as)


def setup_inputs(seed: int = 0) -> dict:
    keys = jax.random.split(jax.random.key(seed), 8)
    tokens = noise(keys[0], (TOKENS, D), 1.0, 6.0, ((0, 256),))
    router_weight = noise(keys[1], (D, EXPERTS), D ** -0.5, 0.125)
    expert_ids_keys = jax.random.split(jax.random.fold_in(keys[2], 1), TOKENS // TOK_DEV)
    expert_ids_turns = jax.random.permutation(jax.random.fold_in(keys[2], 3), TOKENS // TOK_DEV)
    expert_ids = jax.vmap(lambda own, number: assign_block(jax.random.fold_in(keys[2], 2), own, number, TOK_DEV, EXPERTS, TOP, CAP, 2))(expert_ids_keys, expert_ids_turns).reshape((TOKENS, TOP))
    gate_matrix = noise(keys[3], (D, EXPERTS, FF), D ** -0.5, 0.125, ((0, 8), (1, 32)))
    up_matrix = noise(keys[4], (D, EXPERTS, FF), D ** -0.5, 0.125, ((0, 8), (1, 32)))
    down_matrix = noise(keys[5], (D, EXPERTS, FF), FF ** -0.5, 0.3125, ((0, 8), (1, 32)))
    cotangent = noise(keys[6], (TOKENS, D), 0.5, 3.0, ((0, 256),))
    return {"tokens": tokens, "router_weight": router_weight, "expert_ids": expert_ids, "gate_matrix": gate_matrix, "up_matrix": up_matrix, "down_matrix": down_matrix, "cotangent": cotangent}


def reference(tokens, router_weight, expert_ids, gate_matrix, up_matrix, down_matrix, cotangent):
    highest = lax.Precision.HIGHEST
    logits = jnp.dot(tokens, router_weight, preferred_element_type=jnp.float32)
    expert_range = jnp.arange(EXPERTS, dtype=jnp.int32)
    onehot = (expert_ids[:, :, None] == expert_range[None, None, :]).astype(jnp.float32)
    chosen = jnp.sum(onehot * logits[:, None, :], axis=2)
    raised = jnp.exp(chosen)
    gate_weights = raised / jnp.sum(raised, axis=1, keepdims=True)
    group_tokens = TOK_DEV * N_EXPERT
    group_picks = group_tokens * TOP
    group_slots = CAP * N_EXPERT
    grouped_ids = expert_ids.reshape(N_DP, group_picks)
    group_start = (jnp.arange(N_DP, dtype=jnp.int32) * group_picks)[:, None]
    flat_gates = gate_weights.reshape(-1)
    target = cotangent.astype(jnp.float32)
    slot_range = jnp.arange(group_slots, dtype=jnp.int32)

    def expert_step(carry, expert):
        mixed_acc, input_acc, slope_acc = carry

        def locate(row_ids):
            matches = row_ids == expert
            found = jnp.nonzero(matches, size=group_slots, fill_value=0)[0].astype(jnp.int32)
            count = jnp.sum(matches.astype(jnp.int32))
            return found, slot_range < count

        found, live = lax.map(locate, grouped_ids)
        picks = found + group_start
        token_index = picks // TOP
        live_f = live.astype(jnp.float32)
        rows_in = tokens[token_index].astype(jnp.float32) * live_f[..., None]
        gate_w = lax.dynamic_index_in_dim(gate_matrix, expert, 1, False).astype(jnp.float32)
        up_w = lax.dynamic_index_in_dim(up_matrix, expert, 1, False).astype(jnp.float32)
        down_w = lax.dynamic_index_in_dim(down_matrix, expert, 1, False).astype(jnp.float32)
        pre_gate = jnp.einsum('gnd,df->gnf', rows_in, gate_w, precision=highest)
        pre_up = jnp.einsum('gnd,df->gnf', rows_in, up_w, precision=highest)
        hidden = (jax.nn.silu(pre_gate) * pre_up).astype(jnp.bfloat16)
        hidden_f = hidden.astype(jnp.float32)
        outputs = jnp.einsum('gnf,df->gnd', hidden_f, down_w, precision=highest).astype(jnp.bfloat16)
        outputs_f = outputs.astype(jnp.float32)
        gate_rows = flat_gates[picks] * live_f
        mixed_acc = mixed_acc.at[token_index].add(gate_rows[..., None] * outputs_f)
        target_rows = target[token_index]
        slope_acc = slope_acc.at[picks].add(jnp.sum(target_rows * outputs_f, axis=2) * live_f)
        out_slope = (gate_rows[..., None] * target_rows).astype(jnp.bfloat16)
        out_slope_f = out_slope.astype(jnp.float32)
        hidden_slope = jnp.einsum('gnd,df->gnf', out_slope_f, down_w, precision=highest)
        sigmoid_gate = jax.nn.sigmoid(pre_gate)
        activation = pre_gate * sigmoid_gate
        gate_slope = (hidden_slope * pre_up * sigmoid_gate * (1.0 + pre_gate * (1.0 - sigmoid_gate))).astype(jnp.bfloat16)
        up_slope = (hidden_slope * activation).astype(jnp.bfloat16)
        gate_slope_f = gate_slope.astype(jnp.float32)
        up_slope_f = up_slope.astype(jnp.float32)
        pick_slope = (jnp.einsum('gnf,df->gnd', gate_slope_f, gate_w, precision=highest)
                      + jnp.einsum('gnf,df->gnd', up_slope_f, up_w, precision=highest)).astype(jnp.bfloat16)
        input_acc = input_acc.at[token_index].add(pick_slope.astype(jnp.float32) * live_f[..., None])

        def group_total(left, right):
            partial_sums = jnp.einsum('gnd,gnf->gdf', left, right, precision=highest).astype(jnp.bfloat16)
            partial_sums = lax.optimization_barrier(partial_sums)
            return jnp.sum(partial_sums.astype(jnp.float32), axis=0).astype(jnp.bfloat16)

        grad_gate_e = group_total(rows_in, gate_slope_f)
        grad_up_e = group_total(rows_in, up_slope_f)
        grad_down_e = group_total(out_slope_f, hidden_f)
        return (mixed_acc, input_acc, slope_acc), (grad_gate_e, grad_up_e, grad_down_e)

    start_state = (jnp.zeros((TOKENS, D), jnp.float32), jnp.zeros((TOKENS, D), jnp.float32),
                   jnp.zeros((TOKENS * TOP,), jnp.float32))
    final_state, stacked = lax.scan(expert_step, start_state, expert_range)
    mixed_acc, input_acc, slope_acc = final_state
    gate_slope_all = slope_acc.reshape(TOKENS, TOP)
    centred = gate_slope_all - jnp.sum(gate_weights * gate_slope_all, axis=1, keepdims=True)
    choice_slope = gate_weights * centred
    logit_slope = jnp.sum(onehot * choice_slope[:, :, None], axis=1)
    router_part = jnp.dot(logit_slope, router_weight.astype(jnp.float32).T, precision=highest)
    token_grad = (input_acc + router_part).astype(jnp.bfloat16)
    router_grad = jnp.dot(tokens.astype(jnp.float32).T, logit_slope, precision=highest)
    gate_grad = jnp.transpose(stacked[0], (1, 0, 2))
    up_grad = jnp.transpose(stacked[1], (1, 0, 2))
    down_grad = jnp.transpose(stacked[2], (1, 0, 2))
    return (mixed_acc.astype(jnp.bfloat16), token_grad, gate_grad, up_grad, down_grad, router_grad)
```

```python
import jax
import jax.numpy as jnp
from jax import lax
from jax.sharding import PartitionSpec as P


def shards(tokens, router_weight, expert_ids, gate_matrix, up_matrix, down_matrix, cotangent):
    highest = lax.Precision.HIGHEST
    token_count = tokens.shape[0]
    model_width = tokens.shape[1]
    top_count = expert_ids.shape[1]
    experts_total = router_weight.shape[1]
    owners = lax.axis_size("expert")
    local_experts = gate_matrix.shape[1]
    capacity = 3 * token_count * top_count // (2 * experts_total)
    pick_count = token_count * top_count
    slot_count = experts_total * capacity
    logits = jnp.dot(tokens, router_weight, preferred_element_type=jnp.float32)
    expert_range = lax.iota(jnp.int32, experts_total)
    onehot = (expert_ids[:, :, None] == expert_range[None, None, :]).astype(jnp.float32)
    chosen = jnp.sum(onehot * logits[:, None, :], axis=2)
    raised = jnp.exp(chosen)
    gate_weights = raised / jnp.sum(raised, axis=1, keepdims=True)
    flat_ids = expert_ids.reshape(pick_count)
    flat_hits = (flat_ids[:, None] == expert_range[None, :]).astype(jnp.bfloat16)
    pick_range = lax.iota(jnp.int32, pick_count)
    before = (pick_range[None, :] < pick_range[:, None]).astype(jnp.bfloat16)
    earlier = jnp.dot(before, flat_hits, preferred_element_type=jnp.float32)
    slot_index = jnp.sum(earlier * flat_hits.astype(jnp.float32), axis=1).astype(jnp.int32)
    position = (flat_ids * capacity + slot_index).reshape(token_count, top_count)
    slot_range = lax.iota(jnp.int32, slot_count)
    slot_hits = position[None, :, :] == slot_range[:, None, None]
    slot_token = jnp.any(slot_hits, axis=2)
    slot_token_b = slot_token.astype(jnp.bfloat16)
    slot_gate = jnp.sum(jnp.where(slot_hits, gate_weights[None, :, :], 0.0), axis=(1, 2))
    send_tokens = (
        jnp.dot(slot_token_b, tokens, preferred_element_type=jnp.float32)
        .astype(jnp.bfloat16)
        .reshape(owners, local_experts, capacity, model_width)
    )
    target = cotangent.astype(jnp.float32)
    slot_target = jnp.dot(slot_token_b, cotangent, preferred_element_type=jnp.float32)
    send_slopes = (
        (slot_gate[:, None] * slot_target)
        .astype(jnp.bfloat16)
        .reshape(owners, local_experts, capacity, model_width)
    )
    gate_full, up_full, down_full = (
        lax.all_gather(gate_matrix, "dp", axis=0, tiled=True),
        lax.all_gather(up_matrix, "dp", axis=0, tiled=True),
        lax.all_gather(down_matrix, "dp", axis=0, tiled=True),
    )
    received = lax.all_to_all(send_tokens, "expert", split_axis=0, concat_axis=0, tiled=True)
    pre_gate = jnp.einsum("sjcd,djf->sjcf", received, gate_full, preferred_element_type=jnp.float32)
    pre_up = jnp.einsum("sjcd,djf->sjcf", received, up_full, preferred_element_type=jnp.float32)
    expert_hidden = (jax.nn.silu(pre_gate) * pre_up).astype(jnp.bfloat16)
    outputs = jnp.einsum(
        "sjcf,djf->sjcd", expert_hidden, down_full, preferred_element_type=jnp.float32
    ).astype(jnp.bfloat16)
    hidden = expert_hidden
    returned = lax.all_to_all(outputs, "expert", split_axis=0, concat_axis=0, tiled=True)
    returned_rows = returned.reshape(slot_count, model_width)
    slot_mix = jnp.where(slot_token.T, slot_gate[None, :], 0.0)
    mix_high = slot_mix.astype(jnp.bfloat16)
    mix_low = (slot_mix - mix_high.astype(jnp.float32)).astype(jnp.bfloat16)
    mixed_out = (
        jnp.dot(mix_high, returned_rows, preferred_element_type=jnp.float32)
        + jnp.dot(mix_low, returned_rows, preferred_element_type=jnp.float32)
    ).astype(jnp.bfloat16)
    token_slot_slope = lax.dot_general(
        cotangent, returned_rows, (((1,), (1,)), ((), ())), preferred_element_type=jnp.float32
    )
    gate_slope_all = jnp.take_along_axis(token_slot_slope, position, axis=1)
    centred = gate_slope_all - jnp.sum(gate_weights * gate_slope_all, axis=1, keepdims=True)
    choice_slope = gate_weights * centred
    logit_slope = jnp.sum(onehot * choice_slope[:, :, None], axis=1)
    router_local = jnp.dot(tokens.astype(jnp.float32).T, logit_slope, precision=highest)
    send_slopes, router_local = lax.optimization_barrier((send_slopes, router_local))
    row_parts = router_local.reshape(owners, model_width // owners, experts_total)
    row_parts = lax.all_to_all(row_parts, "expert", split_axis=0, concat_axis=0, tiled=True)
    row_block = lax.psum(jnp.sum(row_parts, axis=0), "dp")
    row_copies = jnp.broadcast_to(row_block[None], (owners,) + row_block.shape)
    router_grad = lax.all_to_all(
        row_copies, "expert", split_axis=0, concat_axis=0, tiled=True
    ).reshape(model_width, experts_total)
    slopes_in = lax.all_to_all(send_slopes, "expert", split_axis=0, concat_axis=0, tiled=True)
    hidden_slope = jnp.einsum(
        "sjcd,djf->sjcf", slopes_in, down_full, preferred_element_type=jnp.float32
    )
    sigmoid_gate = jax.nn.sigmoid(pre_gate)
    activation = pre_gate * sigmoid_gate
    expert_gate_slope = (
        hidden_slope * pre_up * sigmoid_gate * (1.0 + pre_gate * (1.0 - sigmoid_gate))
    ).astype(jnp.bfloat16)
    expert_up_slope = (hidden_slope * activation).astype(jnp.bfloat16)
    pick_slope = (
        jnp.einsum(
            "sjcf,djf->sjcd", expert_gate_slope, gate_full, preferred_element_type=jnp.float32
        )
        + jnp.einsum("sjcf,djf->sjcd", expert_up_slope, up_full, preferred_element_type=jnp.float32)
    ).astype(jnp.bfloat16)
    gate_slope, up_slope = (expert_gate_slope, expert_up_slope)
    slopes_back = lax.all_to_all(pick_slope, "expert", split_axis=0, concat_axis=0, tiled=True)
    back_rows = slopes_back.reshape(slot_count, model_width)
    input_sum = lax.dot_general(
        slot_token_b, back_rows, (((0,), (0,)), ((), ())), preferred_element_type=jnp.float32
    )
    router_part = jnp.dot(logit_slope, router_weight.astype(jnp.float32).T, precision=highest)
    token_grad = (input_sum + router_part).astype(jnp.bfloat16)
    grad_gate_rows = jnp.einsum(
        "sjcd,sjcf->djf", received, gate_slope, preferred_element_type=jnp.float32
    )
    grad_up_rows = jnp.einsum(
        "sjcd,sjcf->djf", received, up_slope, preferred_element_type=jnp.float32
    )
    grad_down_rows = jnp.einsum(
        "sjcd,sjcf->djf", slopes_in, hidden, preferred_element_type=jnp.float32
    )
    summed = lax.psum_scatter(
        jnp.stack([grad_gate_rows, grad_up_rows, grad_down_rows], axis=1).astype(jnp.bfloat16),
        "dp",
        scatter_dimension=0,
        tiled=True,
    )
    gate_grad = summed[:, 0]
    up_grad = summed[:, 1]
    down_grad = summed[:, 2]
    return (mixed_out, token_grad, gate_grad, up_grad, down_grad, router_grad)


def solution(mesh):
    in_specs = (
        P(("dp", "expert"), None),
        P(),
        P(("dp", "expert"), None),
        P("dp", "expert", None),
        P("dp", "expert", None),
        P("dp", "expert", None),
        P(("dp", "expert"), None),
    )
    out_specs = (
        P(("dp", "expert"), None),
        P(("dp", "expert"), None),
        P("dp", "expert", None),
        P("dp", "expert", None),
        P("dp", "expert", None),
        P(),
    )
    return jax.shard_map(shards, mesh=mesh, in_specs=in_specs, out_specs=out_specs, check_vma=False)
```

```python
import jax
import jax.numpy as jnp
from jax import lax
from jax.sharding import PartitionSpec as P


def shards(tokens, router_weight, expert_ids, gate_matrix, up_matrix, down_matrix, cotangent):
    highest = lax.Precision.HIGHEST
    token_count = tokens.shape[0]
    model_width = tokens.shape[1]
    top_count = expert_ids.shape[1]
    experts_total = router_weight.shape[1]
    owners = lax.axis_size("expert")
    local_experts = gate_matrix.shape[1]
    capacity = 3 * token_count * top_count // (2 * experts_total)
    pick_count = token_count * top_count
    slot_count = experts_total * capacity
    logits = jnp.dot(tokens, router_weight, preferred_element_type=jnp.float32)
    expert_range = lax.iota(jnp.int32, experts_total)
    onehot = (expert_ids[:, :, None] == expert_range[None, None, :]).astype(jnp.float32)
    chosen = jnp.sum(onehot * logits[:, None, :], axis=2)
    raised = jnp.exp(chosen)
    gate_weights = raised / jnp.sum(raised, axis=1, keepdims=True)
    flat_ids = expert_ids.reshape(pick_count)
    flat_hits = (flat_ids[:, None] == expert_range[None, :]).astype(jnp.bfloat16)
    pick_range = lax.iota(jnp.int32, pick_count)
    before = (pick_range[None, :] < pick_range[:, None]).astype(jnp.bfloat16)
    earlier = jnp.dot(before, flat_hits, preferred_element_type=jnp.float32)
    slot_index = jnp.sum(earlier * flat_hits.astype(jnp.float32), axis=1).astype(jnp.int32)
    position = (flat_ids * capacity + slot_index).reshape(token_count, top_count)
    slot_range = lax.iota(jnp.int32, slot_count)
    slot_hits = position[None, :, :] == slot_range[:, None, None]
    slot_token = jnp.any(slot_hits, axis=2)
    slot_token_b = slot_token.astype(jnp.bfloat16)
    slot_gate = jnp.sum(jnp.where(slot_hits, gate_weights[None, :, :], 0.0), axis=(1, 2))
    send_tokens = (
        jnp.dot(slot_token_b, tokens, preferred_element_type=jnp.float32)
        .astype(jnp.bfloat16)
        .reshape(owners, local_experts, capacity, model_width)
    )
    slot_target = jnp.dot(slot_token_b, cotangent, preferred_element_type=jnp.float32)
    send_slopes = (
        (slot_gate[:, None] * slot_target)
        .astype(jnp.bfloat16)
        .reshape(owners, local_experts, capacity, model_width)
    )
    gate_full, up_full, down_full = (
        lax.all_gather(gate_matrix, "dp", axis=0, tiled=True),
        lax.all_gather(up_matrix, "dp", axis=0, tiled=True),
        lax.all_gather(down_matrix, "dp", axis=0, tiled=True),
    )
    dispatched = lax.all_to_all(
        jnp.concatenate([send_tokens, send_slopes], axis=3),
        "expert",
        split_axis=0,
        concat_axis=0,
        tiled=True,
    )
    received = dispatched[..., :model_width]
    slopes_in = dispatched[..., model_width:]
    pre_gate = jnp.einsum("sjcd,djf->sjcf", received, gate_full, preferred_element_type=jnp.float32)
    pre_up = jnp.einsum("sjcd,djf->sjcf", received, up_full, preferred_element_type=jnp.float32)
    expert_hidden = (jax.nn.silu(pre_gate) * pre_up).astype(jnp.bfloat16)
    outputs = jnp.einsum(
        "sjcf,djf->sjcd", expert_hidden, down_full, preferred_element_type=jnp.float32
    ).astype(jnp.bfloat16)
    hidden = expert_hidden
    hidden_slope = jnp.einsum(
        "sjcd,djf->sjcf", slopes_in, down_full, preferred_element_type=jnp.float32
    )
    sigmoid_gate = jax.nn.sigmoid(pre_gate)
    activation = pre_gate * sigmoid_gate
    expert_gate_slope = (
        hidden_slope * pre_up * sigmoid_gate * (1.0 + pre_gate * (1.0 - sigmoid_gate))
    ).astype(jnp.bfloat16)
    expert_up_slope = (hidden_slope * activation).astype(jnp.bfloat16)
    pick_slope = (
        jnp.einsum(
            "sjcf,djf->sjcd", expert_gate_slope, gate_full, preferred_element_type=jnp.float32
        )
        + jnp.einsum("sjcf,djf->sjcd", expert_up_slope, up_full, preferred_element_type=jnp.float32)
    ).astype(jnp.bfloat16)
    gate_slope, up_slope = (expert_gate_slope, expert_up_slope)
    gathered = lax.all_to_all(
        jnp.concatenate([outputs, pick_slope], axis=3),
        "expert",
        split_axis=0,
        concat_axis=0,
        tiled=True,
    )
    returned_rows = gathered[..., :model_width].reshape(slot_count, model_width)
    back_rows = gathered[..., model_width:].reshape(slot_count, model_width)
    slot_mix = jnp.where(slot_token.T, slot_gate[None, :], 0.0)
    mix_high = slot_mix.astype(jnp.bfloat16)
    mix_low = (slot_mix - mix_high.astype(jnp.float32)).astype(jnp.bfloat16)
    mixed_out = (
        jnp.dot(mix_high, returned_rows, preferred_element_type=jnp.float32)
        + jnp.dot(mix_low, returned_rows, preferred_element_type=jnp.float32)
    ).astype(jnp.bfloat16)
    token_slot_slope = lax.dot_general(
        cotangent, returned_rows, (((1,), (1,)), ((), ())), preferred_element_type=jnp.float32
    )
    gate_slope_all = jnp.take_along_axis(token_slot_slope, position, axis=1)
    centred = gate_slope_all - jnp.sum(gate_weights * gate_slope_all, axis=1, keepdims=True)
    choice_slope = gate_weights * centred
    logit_slope = jnp.sum(onehot * choice_slope[:, :, None], axis=1)
    router_local = jnp.dot(tokens.astype(jnp.float32).T, logit_slope, precision=highest)
    row_parts = router_local.reshape(owners, model_width // owners, experts_total)
    row_parts = lax.all_to_all(row_parts, "expert", split_axis=0, concat_axis=0, tiled=True)
    row_block = lax.psum(jnp.sum(row_parts, axis=0), "dp")
    row_copies = jnp.broadcast_to(row_block[None], (owners,) + row_block.shape)
    router_grad = lax.all_to_all(
        row_copies, "expert", split_axis=0, concat_axis=0, tiled=True
    ).reshape(model_width, experts_total)
    input_sum = lax.dot_general(
        slot_token_b, back_rows, (((0,), (0,)), ((), ())), preferred_element_type=jnp.float32
    )
    router_part = jnp.dot(logit_slope, router_weight.astype(jnp.float32).T, precision=highest)
    token_grad = (input_sum + router_part).astype(jnp.bfloat16)
    grad_gate_rows = jnp.einsum(
        "sjcd,sjcf->djf", received, gate_slope, preferred_element_type=jnp.float32
    )
    grad_up_rows = jnp.einsum(
        "sjcd,sjcf->djf", received, up_slope, preferred_element_type=jnp.float32
    )
    grad_down_rows = jnp.einsum(
        "sjcd,sjcf->djf", slopes_in, hidden, preferred_element_type=jnp.float32
    )
    summed = lax.psum_scatter(
        jnp.stack([grad_gate_rows, grad_up_rows, grad_down_rows], axis=1).astype(jnp.bfloat16),
        "dp",
        scatter_dimension=0,
        tiled=True,
    )
    gate_grad = summed[:, 0]
    up_grad = summed[:, 1]
    down_grad = summed[:, 2]
    return (mixed_out, token_grad, gate_grad, up_grad, down_grad, router_grad)


def solution(mesh):
    in_specs = (
        P(("dp", "expert"), None),
        P(),
        P(("dp", "expert"), None),
        P("dp", "expert", None),
        P("dp", "expert", None),
        P("dp", "expert", None),
        P(("dp", "expert"), None),
    )
    out_specs = (
        P(("dp", "expert"), None),
        P(("dp", "expert"), None),
        P("dp", "expert", None),
        P("dp", "expert", None),
        P("dp", "expert", None),
        P(),
    )
    return jax.shard_map(shards, mesh=mesh, in_specs=in_specs, out_specs=out_specs, check_vma=False)
```

```python
import jax
import jax.numpy as jnp
from jax import lax
from jax.sharding import PartitionSpec as P


def shards(tokens, router_weight, expert_ids, gate_matrix, up_matrix, down_matrix, cotangent):
    highest = lax.Precision.HIGHEST
    token_count = tokens.shape[0]
    model_width = tokens.shape[1]
    top_count = expert_ids.shape[1]
    experts_total = router_weight.shape[1]
    owners = lax.axis_size("expert")
    local_experts = gate_matrix.shape[1]
    capacity = 3 * token_count * top_count // (2 * experts_total)
    pick_count = token_count * top_count
    slot_count = experts_total * capacity
    logits = jnp.dot(tokens, router_weight, preferred_element_type=jnp.float32)
    expert_range = lax.iota(jnp.int32, experts_total)
    onehot = (expert_ids[:, :, None] == expert_range[None, None, :]).astype(jnp.float32)
    chosen = jnp.sum(onehot * logits[:, None, :], axis=2)
    raised = jnp.exp(chosen)
    gate_weights = raised / jnp.sum(raised, axis=1, keepdims=True)
    flat_ids = expert_ids.reshape(pick_count)
    flat_hits = (flat_ids[:, None] == expert_range[None, :]).astype(jnp.bfloat16)
    pick_range = lax.iota(jnp.int32, pick_count)
    before = (pick_range[None, :] < pick_range[:, None]).astype(jnp.bfloat16)
    earlier = jnp.dot(before, flat_hits, preferred_element_type=jnp.float32)
    slot_index = jnp.sum(earlier * flat_hits.astype(jnp.float32), axis=1).astype(jnp.int32)
    position = (flat_ids * capacity + slot_index).reshape(token_count, top_count)
    slot_range = lax.iota(jnp.int32, slot_count)
    slot_hits = position[None, :, :] == slot_range[:, None, None]
    slot_token = jnp.any(slot_hits, axis=2)
    slot_token_b = slot_token.astype(jnp.bfloat16)
    slot_gate = jnp.sum(jnp.where(slot_hits, gate_weights[None, :, :], 0.0), axis=(1, 2))
    send_tokens = (
        jnp.dot(slot_token_b, tokens, preferred_element_type=jnp.float32)
        .astype(jnp.bfloat16)
        .reshape(owners, local_experts, capacity, model_width)
    )
    slot_target = jnp.dot(slot_token_b, cotangent, preferred_element_type=jnp.float32)
    send_slopes = (
        (slot_gate[:, None] * slot_target)
        .astype(jnp.bfloat16)
        .reshape(owners, local_experts, capacity, model_width)
    )
    gate_full, up_full, down_full = (
        lax.all_gather(gate_matrix, "dp", axis=0, tiled=True),
        lax.all_gather(up_matrix, "dp", axis=0, tiled=True),
        lax.all_gather(down_matrix, "dp", axis=0, tiled=True),
    )
    received = lax.all_to_all(send_tokens, "expert", split_axis=0, concat_axis=0, tiled=True)
    received, send_slopes = lax.optimization_barrier((received, send_slopes))
    slopes_in = lax.all_to_all(send_slopes, "expert", split_axis=0, concat_axis=0, tiled=True)
    pre_gate = jnp.einsum("sjcd,djf->sjcf", received, gate_full, preferred_element_type=jnp.float32)
    pre_up = jnp.einsum("sjcd,djf->sjcf", received, up_full, preferred_element_type=jnp.float32)
    expert_hidden = (jax.nn.silu(pre_gate) * pre_up).astype(jnp.bfloat16)
    outputs = jnp.einsum(
        "sjcf,djf->sjcd", expert_hidden, down_full, preferred_element_type=jnp.float32
    ).astype(jnp.bfloat16)
    hidden = expert_hidden
    outputs, slopes_in = lax.optimization_barrier((outputs, slopes_in))
    returned = lax.all_to_all(outputs, "expert", split_axis=0, concat_axis=0, tiled=True)
    hidden_slope = jnp.einsum(
        "sjcd,djf->sjcf", slopes_in, down_full, preferred_element_type=jnp.float32
    )
    sigmoid_gate = jax.nn.sigmoid(pre_gate)
    activation = pre_gate * sigmoid_gate
    expert_gate_slope = (
        hidden_slope * pre_up * sigmoid_gate * (1.0 + pre_gate * (1.0 - sigmoid_gate))
    ).astype(jnp.bfloat16)
    expert_up_slope = (hidden_slope * activation).astype(jnp.bfloat16)
    pick_slope = (
        jnp.einsum(
            "sjcf,djf->sjcd", expert_gate_slope, gate_full, preferred_element_type=jnp.float32
        )
        + jnp.einsum("sjcf,djf->sjcd", expert_up_slope, up_full, preferred_element_type=jnp.float32)
    ).astype(jnp.bfloat16)
    gate_slope, up_slope = (expert_gate_slope, expert_up_slope)
    pick_slope, returned = lax.optimization_barrier((pick_slope, returned))
    slopes_back = lax.all_to_all(pick_slope, "expert", split_axis=0, concat_axis=0, tiled=True)
    returned_rows = returned.reshape(slot_count, model_width)
    slot_mix = jnp.where(slot_token.T, slot_gate[None, :], 0.0)
    mix_high = slot_mix.astype(jnp.bfloat16)
    mix_low = (slot_mix - mix_high.astype(jnp.float32)).astype(jnp.bfloat16)
    mixed_out = (
        jnp.dot(mix_high, returned_rows, preferred_element_type=jnp.float32)
        + jnp.dot(mix_low, returned_rows, preferred_element_type=jnp.float32)
    ).astype(jnp.bfloat16)
    token_slot_slope = lax.dot_general(
        cotangent, returned_rows, (((1,), (1,)), ((), ())), preferred_element_type=jnp.float32
    )
    gate_slope_all = jnp.take_along_axis(token_slot_slope, position, axis=1)
    centred = gate_slope_all - jnp.sum(gate_weights * gate_slope_all, axis=1, keepdims=True)
    choice_slope = gate_weights * centred
    logit_slope = jnp.sum(onehot * choice_slope[:, :, None], axis=1)
    router_local = jnp.dot(tokens.astype(jnp.float32).T, logit_slope, precision=highest)
    row_parts = router_local.reshape(owners, model_width // owners, experts_total)
    row_parts = lax.all_to_all(row_parts, "expert", split_axis=0, concat_axis=0, tiled=True)
    row_block = lax.psum(jnp.sum(row_parts, axis=0), "dp")
    row_copies = jnp.broadcast_to(row_block[None], (owners,) + row_block.shape)
    router_grad = lax.all_to_all(
        row_copies, "expert", split_axis=0, concat_axis=0, tiled=True
    ).reshape(model_width, experts_total)
    back_rows = slopes_back.reshape(slot_count, model_width)
    input_sum = lax.dot_general(
        slot_token_b, back_rows, (((0,), (0,)), ((), ())), preferred_element_type=jnp.float32
    )
    router_part = jnp.dot(logit_slope, router_weight.astype(jnp.float32).T, precision=highest)
    token_grad = (input_sum + router_part).astype(jnp.bfloat16)
    grad_gate_rows = jnp.einsum(
        "sjcd,sjcf->djf", received, gate_slope, preferred_element_type=jnp.float32
    )
    grad_up_rows = jnp.einsum(
        "sjcd,sjcf->djf", received, up_slope, preferred_element_type=jnp.float32
    )
    grad_down_rows = jnp.einsum(
        "sjcd,sjcf->djf", slopes_in, hidden, preferred_element_type=jnp.float32
    )
    summed = lax.psum_scatter(
        jnp.stack([grad_gate_rows, grad_up_rows, grad_down_rows], axis=1).astype(jnp.bfloat16),
        "dp",
        scatter_dimension=0,
        tiled=True,
    )
    gate_grad = summed[:, 0]
    up_grad = summed[:, 1]
    down_grad = summed[:, 2]
    return (mixed_out, token_grad, gate_grad, up_grad, down_grad, router_grad)


def solution(mesh):
    in_specs = (
        P(("dp", "expert"), None),
        P(),
        P(("dp", "expert"), None),
        P("dp", "expert", None),
        P("dp", "expert", None),
        P("dp", "expert", None),
        P(("dp", "expert"), None),
    )
    out_specs = (
        P(("dp", "expert"), None),
        P(("dp", "expert"), None),
        P("dp", "expert", None),
        P("dp", "expert", None),
        P("dp", "expert", None),
        P(),
    )
    return jax.shard_map(shards, mesh=mesh, in_specs=in_specs, out_specs=out_specs, check_vma=False)
```

```python
import jax
import jax.numpy as jnp
from jax import lax
from jax.sharding import PartitionSpec as P


def shards(tokens, router_weight, expert_ids, gate_matrix, up_matrix, down_matrix, cotangent):
    highest = lax.Precision.HIGHEST
    token_count = tokens.shape[0]
    model_width = tokens.shape[1]
    top_count = expert_ids.shape[1]
    experts_total = router_weight.shape[1]
    owners = lax.axis_size("expert")
    local_experts = gate_matrix.shape[1]
    capacity = 3 * token_count * top_count // (2 * experts_total)
    pick_count = token_count * top_count
    slot_count = experts_total * capacity
    logits = jnp.dot(tokens, router_weight, preferred_element_type=jnp.float32)
    expert_range = lax.iota(jnp.int32, experts_total)
    onehot = (expert_ids[:, :, None] == expert_range[None, None, :]).astype(jnp.float32)
    chosen = jnp.sum(onehot * logits[:, None, :], axis=2)
    raised = jnp.exp(chosen)
    gate_weights = raised / jnp.sum(raised, axis=1, keepdims=True)
    flat_ids = expert_ids.reshape(pick_count)
    flat_hits = (flat_ids[:, None] == expert_range[None, :]).astype(jnp.bfloat16)
    pick_range = lax.iota(jnp.int32, pick_count)
    before = (pick_range[None, :] < pick_range[:, None]).astype(jnp.bfloat16)
    earlier = jnp.dot(before, flat_hits, preferred_element_type=jnp.float32)
    slot_index = jnp.sum(earlier * flat_hits.astype(jnp.float32), axis=1).astype(jnp.int32)
    position = (flat_ids * capacity + slot_index).reshape(token_count, top_count)
    slot_range = lax.iota(jnp.int32, slot_count)
    slot_hits = position[None, :, :] == slot_range[:, None, None]
    slot_token = jnp.any(slot_hits, axis=2)
    slot_token_b = slot_token.astype(jnp.bfloat16)
    slot_gate = jnp.sum(jnp.where(slot_hits, gate_weights[None, :, :], 0.0), axis=(1, 2))
    send_tokens = (
        jnp.dot(slot_token_b, tokens, preferred_element_type=jnp.float32)
        .astype(jnp.bfloat16)
        .reshape(owners, local_experts, capacity, model_width)
    )
    slot_target = jnp.dot(slot_token_b, cotangent, preferred_element_type=jnp.float32)
    send_slopes = (
        (slot_gate[:, None] * slot_target)
        .astype(jnp.bfloat16)
        .reshape(owners, local_experts, capacity, model_width)
    )
    weights_full = lax.all_gather(
        jnp.stack([gate_matrix, up_matrix, down_matrix], axis=0), "dp", axis=1, tiled=True
    )
    gate_full, up_full, down_full = weights_full[0], weights_full[1], weights_full[2]
    received = lax.all_to_all(send_tokens, "expert", split_axis=0, concat_axis=0, tiled=True)
    received, send_slopes = lax.optimization_barrier((received, send_slopes))
    slopes_in = lax.all_to_all(send_slopes, "expert", split_axis=0, concat_axis=0, tiled=True)
    pre_gate = jnp.einsum("sjcd,djf->sjcf", received, gate_full, preferred_element_type=jnp.float32)
    pre_up = jnp.einsum("sjcd,djf->sjcf", received, up_full, preferred_element_type=jnp.float32)
    expert_hidden = (jax.nn.silu(pre_gate) * pre_up).astype(jnp.bfloat16)
    outputs = jnp.einsum(
        "sjcf,djf->sjcd", expert_hidden, down_full, preferred_element_type=jnp.float32
    ).astype(jnp.bfloat16)
    hidden = expert_hidden
    outputs, slopes_in = lax.optimization_barrier((outputs, slopes_in))
    returned = lax.all_to_all(outputs, "expert", split_axis=0, concat_axis=0, tiled=True)
    hidden_slope = jnp.einsum(
        "sjcd,djf->sjcf", slopes_in, down_full, preferred_element_type=jnp.float32
    )
    sigmoid_gate = jax.nn.sigmoid(pre_gate)
    activation = pre_gate * sigmoid_gate
    expert_gate_slope = (
        hidden_slope * pre_up * sigmoid_gate * (1.0 + pre_gate * (1.0 - sigmoid_gate))
    ).astype(jnp.bfloat16)
    expert_up_slope = (hidden_slope * activation).astype(jnp.bfloat16)
    pick_slope = (
        jnp.einsum(
            "sjcf,djf->sjcd", expert_gate_slope, gate_full, preferred_element_type=jnp.float32
        )
        + jnp.einsum("sjcf,djf->sjcd", expert_up_slope, up_full, preferred_element_type=jnp.float32)
    ).astype(jnp.bfloat16)
    gate_slope, up_slope = (expert_gate_slope, expert_up_slope)
    pick_slope, returned = lax.optimization_barrier((pick_slope, returned))
    slopes_back = lax.all_to_all(pick_slope, "expert", split_axis=0, concat_axis=0, tiled=True)
    returned_rows = returned.reshape(slot_count, model_width)
    slot_mix = jnp.where(slot_token.T, slot_gate[None, :], 0.0)
    mix_high = slot_mix.astype(jnp.bfloat16)
    mix_low = (slot_mix - mix_high.astype(jnp.float32)).astype(jnp.bfloat16)
    mixed_out = (
        jnp.dot(mix_high, returned_rows, preferred_element_type=jnp.float32)
        + jnp.dot(mix_low, returned_rows, preferred_element_type=jnp.float32)
    ).astype(jnp.bfloat16)
    token_slot_slope = lax.dot_general(
        cotangent, returned_rows, (((1,), (1,)), ((), ())), preferred_element_type=jnp.float32
    )
    gate_slope_all = jnp.take_along_axis(token_slot_slope, position, axis=1)
    centred = gate_slope_all - jnp.sum(gate_weights * gate_slope_all, axis=1, keepdims=True)
    choice_slope = gate_weights * centred
    logit_slope = jnp.sum(onehot * choice_slope[:, :, None], axis=1)
    router_local = jnp.dot(tokens.astype(jnp.float32).T, logit_slope, precision=highest)
    row_parts = router_local.reshape(owners, model_width // owners, experts_total)
    row_parts = lax.all_to_all(row_parts, "expert", split_axis=0, concat_axis=0, tiled=True)
    row_block = lax.psum(jnp.sum(row_parts, axis=0), "dp")
    row_copies = jnp.broadcast_to(row_block[None], (owners,) + row_block.shape)
    router_grad = lax.all_to_all(
        row_copies, "expert", split_axis=0, concat_axis=0, tiled=True
    ).reshape(model_width, experts_total)
    back_rows = slopes_back.reshape(slot_count, model_width)
    input_sum = lax.dot_general(
        slot_token_b, back_rows, (((0,), (0,)), ((), ())), preferred_element_type=jnp.float32
    )
    router_part = jnp.dot(logit_slope, router_weight.astype(jnp.float32).T, precision=highest)
    token_grad = (input_sum + router_part).astype(jnp.bfloat16)
    grad_gate_rows = jnp.einsum(
        "sjcd,sjcf->djf", received, gate_slope, preferred_element_type=jnp.float32
    )
    grad_up_rows = jnp.einsum(
        "sjcd,sjcf->djf", received, up_slope, preferred_element_type=jnp.float32
    )
    grad_down_rows = jnp.einsum(
        "sjcd,sjcf->djf", slopes_in, hidden, preferred_element_type=jnp.float32
    )
    summed = lax.psum_scatter(
        jnp.stack([grad_gate_rows, grad_up_rows, grad_down_rows], axis=1).astype(jnp.bfloat16),
        "dp",
        scatter_dimension=0,
        tiled=True,
    )
    gate_grad = summed[:, 0]
    up_grad = summed[:, 1]
    down_grad = summed[:, 2]
    return (mixed_out, token_grad, gate_grad, up_grad, down_grad, router_grad)


def solution(mesh):
    in_specs = (
        P(("dp", "expert"), None),
        P(),
        P(("dp", "expert"), None),
        P("dp", "expert", None),
        P("dp", "expert", None),
        P("dp", "expert", None),
        P(("dp", "expert"), None),
    )
    out_specs = (
        P(("dp", "expert"), None),
        P(("dp", "expert"), None),
        P("dp", "expert", None),
        P("dp", "expert", None),
        P("dp", "expert", None),
        P(),
    )
    return jax.shard_map(shards, mesh=mesh, in_specs=in_specs, out_specs=out_specs, check_vma=False)
```

```python
import jax
import jax.numpy as jnp
from jax import lax
from jax.sharding import PartitionSpec as P


def shards(tokens, router_weight, expert_ids, gate_matrix, up_matrix, down_matrix, cotangent):
    highest = lax.Precision.HIGHEST
    token_count = tokens.shape[0]
    model_width = tokens.shape[1]
    top_count = expert_ids.shape[1]
    experts_total = router_weight.shape[1]
    owners = lax.axis_size("expert")
    local_experts = gate_matrix.shape[1]
    capacity = 3 * token_count * top_count // (2 * experts_total)
    pick_count = token_count * top_count
    slot_count = experts_total * capacity
    logits = jnp.dot(tokens, router_weight, preferred_element_type=jnp.float32)
    expert_range = lax.iota(jnp.int32, experts_total)
    onehot = (expert_ids[:, :, None] == expert_range[None, None, :]).astype(jnp.float32)
    chosen = jnp.sum(onehot * logits[:, None, :], axis=2)
    raised = jnp.exp(chosen)
    gate_weights = raised / jnp.sum(raised, axis=1, keepdims=True)
    flat_ids = expert_ids.reshape(pick_count)
    flat_hits = (flat_ids[:, None] == expert_range[None, :]).astype(jnp.bfloat16)
    pick_range = lax.iota(jnp.int32, pick_count)
    before = (pick_range[None, :] < pick_range[:, None]).astype(jnp.bfloat16)
    earlier = jnp.dot(before, flat_hits, preferred_element_type=jnp.float32)
    slot_index = jnp.sum(earlier * flat_hits.astype(jnp.float32), axis=1).astype(jnp.int32)
    position = (flat_ids * capacity + slot_index).reshape(token_count, top_count)
    slot_range = lax.iota(jnp.int32, slot_count)
    slot_hits = position[None, :, :] == slot_range[:, None, None]
    slot_token = jnp.any(slot_hits, axis=2)
    slot_token_b = slot_token.astype(jnp.bfloat16)
    slot_gate = jnp.sum(jnp.where(slot_hits, gate_weights[None, :, :], 0.0), axis=(1, 2))
    send_tokens = (
        jnp.dot(slot_token_b, tokens, preferred_element_type=jnp.float32)
        .astype(jnp.bfloat16)
        .reshape(owners, local_experts, capacity, model_width)
    )
    slot_target = jnp.dot(slot_token_b, cotangent, preferred_element_type=jnp.float32)
    send_slopes = (
        (slot_gate[:, None] * slot_target)
        .astype(jnp.bfloat16)
        .reshape(owners, local_experts, capacity, model_width)
    )
    weights_full = lax.all_gather(
        jnp.stack([gate_matrix, up_matrix, down_matrix], axis=0), "dp", axis=1, tiled=True
    )
    gate_full, up_full, down_full = weights_full[0], weights_full[1], weights_full[2]
    received = lax.all_to_all(send_tokens, "expert", split_axis=0, concat_axis=0, tiled=True)
    received, send_slopes = lax.optimization_barrier((received, send_slopes))
    slopes_in = lax.all_to_all(send_slopes, "expert", split_axis=0, concat_axis=0, tiled=True)
    pre_gate = jnp.einsum("sjcd,djf->sjcf", received, gate_full, preferred_element_type=jnp.float32)
    pre_up = jnp.einsum("sjcd,djf->sjcf", received, up_full, preferred_element_type=jnp.float32)
    expert_hidden = (jax.nn.silu(pre_gate) * pre_up).astype(jnp.bfloat16)
    outputs = jnp.einsum(
        "sjcf,djf->sjcd", expert_hidden, down_full, preferred_element_type=jnp.float32
    ).astype(jnp.bfloat16)
    hidden = expert_hidden
    outputs, slopes_in = lax.optimization_barrier((outputs, slopes_in))
    returned = lax.all_to_all(outputs, "expert", split_axis=0, concat_axis=0, tiled=True)
    hidden_slope = jnp.einsum(
        "sjcd,djf->sjcf", slopes_in, down_full, preferred_element_type=jnp.float32
    )
    sigmoid_gate = jax.nn.sigmoid(pre_gate)
    activation = pre_gate * sigmoid_gate
    expert_gate_slope = (
        hidden_slope * pre_up * sigmoid_gate * (1.0 + pre_gate * (1.0 - sigmoid_gate))
    ).astype(jnp.bfloat16)
    expert_up_slope = (hidden_slope * activation).astype(jnp.bfloat16)
    pick_slope = (
        jnp.einsum(
            "sjcf,djf->sjcd", expert_gate_slope, gate_full, preferred_element_type=jnp.float32
        )
        + jnp.einsum("sjcf,djf->sjcd", expert_up_slope, up_full, preferred_element_type=jnp.float32)
    ).astype(jnp.bfloat16)
    gate_slope, up_slope = (expert_gate_slope, expert_up_slope)
    pick_slope, returned = lax.optimization_barrier((pick_slope, returned))
    slopes_back = lax.all_to_all(pick_slope, "expert", split_axis=0, concat_axis=0, tiled=True)
    returned_rows = returned.reshape(slot_count, model_width)
    slot_mix = jnp.where(slot_token.T, slot_gate[None, :], 0.0)
    mix_high = slot_mix.astype(jnp.bfloat16)
    mix_low = (slot_mix - mix_high.astype(jnp.float32)).astype(jnp.bfloat16)
    mixed_out = (
        jnp.dot(mix_high, returned_rows, preferred_element_type=jnp.float32)
        + jnp.dot(mix_low, returned_rows, preferred_element_type=jnp.float32)
    ).astype(jnp.bfloat16)
    token_slot_slope = lax.dot_general(
        cotangent, returned_rows, (((1,), (1,)), ((), ())), preferred_element_type=jnp.float32
    )
    gate_slope_all = jnp.take_along_axis(token_slot_slope, position, axis=1)
    centred = gate_slope_all - jnp.sum(gate_weights * gate_slope_all, axis=1, keepdims=True)
    choice_slope = gate_weights * centred
    logit_slope = jnp.sum(onehot * choice_slope[:, :, None], axis=1)
    router_local = jnp.dot(tokens.astype(jnp.float32).T, logit_slope, precision=highest)
    slopes_back, router_local = lax.optimization_barrier((slopes_back, router_local))
    row_parts = router_local.reshape(owners, model_width // owners, experts_total)
    row_parts = lax.all_to_all(row_parts, "expert", split_axis=0, concat_axis=0, tiled=True)
    row_block = lax.psum(jnp.sum(row_parts, axis=0), "dp")
    row_copies = jnp.broadcast_to(row_block[None], (owners,) + row_block.shape)
    router_grad = lax.all_to_all(
        row_copies, "expert", split_axis=0, concat_axis=0, tiled=True
    ).reshape(model_width, experts_total)
    back_rows = slopes_back.reshape(slot_count, model_width)
    input_sum = lax.dot_general(
        slot_token_b, back_rows, (((0,), (0,)), ((), ())), preferred_element_type=jnp.float32
    )
    router_part = jnp.dot(logit_slope, router_weight.astype(jnp.float32).T, precision=highest)
    token_grad = (input_sum + router_part).astype(jnp.bfloat16)
    grad_gate_rows = jnp.einsum(
        "sjcd,sjcf->djf", received, gate_slope, preferred_element_type=jnp.float32
    )
    grad_up_rows = jnp.einsum(
        "sjcd,sjcf->djf", received, up_slope, preferred_element_type=jnp.float32
    )
    grad_down_rows = jnp.einsum(
        "sjcd,sjcf->djf", slopes_in, hidden, preferred_element_type=jnp.float32
    )
    summed = lax.psum_scatter(
        jnp.stack([grad_gate_rows, grad_up_rows, grad_down_rows], axis=1).astype(jnp.bfloat16),
        "dp",
        scatter_dimension=0,
        tiled=True,
    )
    gate_grad = summed[:, 0]
    up_grad = summed[:, 1]
    down_grad = summed[:, 2]
    return (mixed_out, token_grad, gate_grad, up_grad, down_grad, router_grad)


def solution(mesh):
    in_specs = (
        P(("dp", "expert"), None),
        P(),
        P(("dp", "expert"), None),
        P("dp", "expert", None),
        P("dp", "expert", None),
        P("dp", "expert", None),
        P(("dp", "expert"), None),
    )
    out_specs = (
        P(("dp", "expert"), None),
        P(("dp", "expert"), None),
        P("dp", "expert", None),
        P("dp", "expert", None),
        P("dp", "expert", None),
        P(),
    )
    return jax.shard_map(shards, mesh=mesh, in_specs=in_specs, out_specs=out_specs, check_vma=False)
```

```python
import jax
import jax.numpy as jnp
from jax import lax
from jax.sharding import PartitionSpec as P


def shards(tokens, router_weight, expert_ids, gate_matrix, up_matrix, down_matrix, cotangent):
    highest = lax.Precision.HIGHEST
    token_count = tokens.shape[0]
    model_width = tokens.shape[1]
    top_count = expert_ids.shape[1]
    experts_total = router_weight.shape[1]
    owners = lax.axis_size("expert")
    local_experts = gate_matrix.shape[1]
    capacity = 3 * token_count * top_count // (2 * experts_total)
    pick_count = token_count * top_count
    slot_count = experts_total * capacity
    logits = jnp.dot(tokens, router_weight, preferred_element_type=jnp.float32)
    expert_range = lax.iota(jnp.int32, experts_total)
    onehot = (expert_ids[:, :, None] == expert_range[None, None, :]).astype(jnp.float32)
    chosen = jnp.sum(onehot * logits[:, None, :], axis=2)
    raised = jnp.exp(chosen)
    gate_weights = raised / jnp.sum(raised, axis=1, keepdims=True)
    flat_ids = expert_ids.reshape(pick_count)
    flat_hits = (flat_ids[:, None] == expert_range[None, :]).astype(jnp.bfloat16)
    pick_range = lax.iota(jnp.int32, pick_count)
    before = (pick_range[None, :] < pick_range[:, None]).astype(jnp.bfloat16)
    earlier = jnp.dot(before, flat_hits, preferred_element_type=jnp.float32)
    slot_index = jnp.sum(earlier * flat_hits.astype(jnp.float32), axis=1).astype(jnp.int32)
    position = (flat_ids * capacity + slot_index).reshape(token_count, top_count)
    slot_range = lax.iota(jnp.int32, slot_count)
    slot_hits = position[None, :, :] == slot_range[:, None, None]
    slot_token = jnp.any(slot_hits, axis=2)
    slot_token_b = slot_token.astype(jnp.bfloat16)
    slot_gate = jnp.sum(jnp.where(slot_hits, gate_weights[None, :, :], 0.0), axis=(1, 2))
    send_tokens = (
        jnp.dot(slot_token_b, tokens, preferred_element_type=jnp.float32)
        .astype(jnp.bfloat16)
        .reshape(owners, local_experts, capacity, model_width)
    )
    slot_target = jnp.dot(slot_token_b, cotangent, preferred_element_type=jnp.float32)
    send_slopes = (
        (slot_gate[:, None] * slot_target)
        .astype(jnp.bfloat16)
        .reshape(owners, local_experts, capacity, model_width)
    )
    weights_full = lax.all_gather(
        jnp.stack([gate_matrix, up_matrix, down_matrix], axis=0), "dp", axis=1, tiled=True
    )
    gate_full, up_full, down_full = weights_full[0], weights_full[1], weights_full[2]
    received = lax.all_to_all(send_tokens, "expert", split_axis=0, concat_axis=0, tiled=True)
    received, send_slopes = lax.optimization_barrier((received, send_slopes))
    slopes_in = lax.all_to_all(send_slopes, "expert", split_axis=0, concat_axis=0, tiled=True)
    pre_gate = jnp.einsum("sjcd,djf->sjcf", received, gate_full, preferred_element_type=jnp.float32)
    pre_up = jnp.einsum("sjcd,djf->sjcf", received, up_full, preferred_element_type=jnp.float32)
    expert_hidden = (jax.nn.silu(pre_gate) * pre_up).astype(jnp.bfloat16)
    outputs = jnp.einsum(
        "sjcf,djf->sjcd", expert_hidden, down_full, preferred_element_type=jnp.float32
    ).astype(jnp.bfloat16)
    hidden = expert_hidden
    outputs, slopes_in = lax.optimization_barrier((outputs, slopes_in))
    returned = lax.all_to_all(outputs, "expert", split_axis=0, concat_axis=0, tiled=True)
    hidden_slope = jnp.einsum(
        "sjcd,djf->sjcf", slopes_in, down_full, preferred_element_type=jnp.float32
    )
    sigmoid_gate = jax.nn.sigmoid(pre_gate)
    activation = pre_gate * sigmoid_gate
    expert_gate_slope = (
        hidden_slope * pre_up * sigmoid_gate * (1.0 + pre_gate * (1.0 - sigmoid_gate))
    ).astype(jnp.bfloat16)
    expert_up_slope = (hidden_slope * activation).astype(jnp.bfloat16)
    pick_slope = (
        jnp.einsum(
            "sjcf,djf->sjcd", expert_gate_slope, gate_full, preferred_element_type=jnp.float32
        )
        + jnp.einsum("sjcf,djf->sjcd", expert_up_slope, up_full, preferred_element_type=jnp.float32)
    ).astype(jnp.bfloat16)
    gate_slope, up_slope = (expert_gate_slope, expert_up_slope)
    pick_slope, returned = lax.optimization_barrier((pick_slope, returned))
    slopes_back = lax.all_to_all(pick_slope, "expert", split_axis=0, concat_axis=0, tiled=True)
    returned_rows = returned.reshape(slot_count, model_width)
    slot_mix = jnp.where(slot_token.T, slot_gate[None, :], 0.0)
    mix_high = slot_mix.astype(jnp.bfloat16)
    mix_low = (slot_mix - mix_high.astype(jnp.float32)).astype(jnp.bfloat16)
    mixed_out = (
        jnp.dot(mix_high, returned_rows, preferred_element_type=jnp.float32)
        + jnp.dot(mix_low, returned_rows, preferred_element_type=jnp.float32)
    ).astype(jnp.bfloat16)
    token_slot_slope = lax.dot_general(
        cotangent, returned_rows, (((1,), (1,)), ((), ())), preferred_element_type=jnp.float32
    )
    gate_slope_all = jnp.take_along_axis(token_slot_slope, position, axis=1)
    centred = gate_slope_all - jnp.sum(gate_weights * gate_slope_all, axis=1, keepdims=True)
    choice_slope = gate_weights * centred
    logit_slope = jnp.sum(onehot * choice_slope[:, :, None], axis=1)
    router_local = jnp.dot(tokens.astype(jnp.float32).T, logit_slope, precision=highest)
    router_group = lax.psum(router_local, "dp")
    slopes_back, router_group = lax.optimization_barrier((slopes_back, router_group))
    row_parts = router_group.reshape(owners, model_width // owners, experts_total)
    row_parts = lax.all_to_all(row_parts, "expert", split_axis=0, concat_axis=0, tiled=True)
    row_block = jnp.sum(row_parts, axis=0)
    row_copies = jnp.broadcast_to(row_block[None], (owners,) + row_block.shape)
    router_grad = lax.all_to_all(
        row_copies, "expert", split_axis=0, concat_axis=0, tiled=True
    ).reshape(model_width, experts_total)
    back_rows = slopes_back.reshape(slot_count, model_width)
    input_sum = lax.dot_general(
        slot_token_b, back_rows, (((0,), (0,)), ((), ())), preferred_element_type=jnp.float32
    )
    router_part = jnp.dot(logit_slope, router_weight.astype(jnp.float32).T, precision=highest)
    token_grad = (input_sum + router_part).astype(jnp.bfloat16)
    grad_gate_rows = jnp.einsum(
        "sjcd,sjcf->djf", received, gate_slope, preferred_element_type=jnp.float32
    )
    grad_up_rows = jnp.einsum(
        "sjcd,sjcf->djf", received, up_slope, preferred_element_type=jnp.float32
    )
    grad_down_rows = jnp.einsum(
        "sjcd,sjcf->djf", slopes_in, hidden, preferred_element_type=jnp.float32
    )
    summed = lax.psum_scatter(
        jnp.stack([grad_gate_rows, grad_up_rows, grad_down_rows], axis=1).astype(jnp.bfloat16),
        "dp",
        scatter_dimension=0,
        tiled=True,
    )
    gate_grad = summed[:, 0]
    up_grad = summed[:, 1]
    down_grad = summed[:, 2]
    return (mixed_out, token_grad, gate_grad, up_grad, down_grad, router_grad)


def solution(mesh):
    in_specs = (
        P(("dp", "expert"), None),
        P(),
        P(("dp", "expert"), None),
        P("dp", "expert", None),
        P("dp", "expert", None),
        P("dp", "expert", None),
        P(("dp", "expert"), None),
    )
    out_specs = (
        P(("dp", "expert"), None),
        P(("dp", "expert"), None),
        P("dp", "expert", None),
        P("dp", "expert", None),
        P("dp", "expert", None),
        P(),
    )
    return jax.shard_map(shards, mesh=mesh, in_specs=in_specs, out_specs=out_specs, check_vma=False)
```

```python
import jax
import jax.numpy as jnp
from jax import lax
from jax.sharding import PartitionSpec as P


def shards(tokens, router_weight, expert_ids, gate_matrix, up_matrix, down_matrix, cotangent):
    highest = lax.Precision.HIGHEST
    token_count = tokens.shape[0]
    model_width = tokens.shape[1]
    top_count = expert_ids.shape[1]
    experts_total = router_weight.shape[1]
    owners = lax.axis_size("expert")
    local_experts = gate_matrix.shape[1]
    capacity = 3 * token_count * top_count // (2 * experts_total)
    pick_count = token_count * top_count
    slot_count = experts_total * capacity
    logits = jnp.dot(tokens, router_weight, preferred_element_type=jnp.float32)
    expert_range = lax.iota(jnp.int32, experts_total)
    onehot = (expert_ids[:, :, None] == expert_range[None, None, :]).astype(jnp.float32)
    chosen = jnp.sum(onehot * logits[:, None, :], axis=2)
    raised = jnp.exp(chosen)
    gate_weights = raised / jnp.sum(raised, axis=1, keepdims=True)
    flat_ids = expert_ids.reshape(pick_count)
    flat_hits = (flat_ids[:, None] == expert_range[None, :]).astype(jnp.bfloat16)
    pick_range = lax.iota(jnp.int32, pick_count)
    before = (pick_range[None, :] < pick_range[:, None]).astype(jnp.bfloat16)
    earlier = jnp.dot(before, flat_hits, preferred_element_type=jnp.float32)
    slot_index = jnp.sum(earlier * flat_hits.astype(jnp.float32), axis=1).astype(jnp.int32)
    position = (flat_ids * capacity + slot_index).reshape(token_count, top_count)
    slot_range = lax.iota(jnp.int32, slot_count)
    slot_hits = position[None, :, :] == slot_range[:, None, None]
    slot_token = jnp.any(slot_hits, axis=2)
    slot_token_b = slot_token.astype(jnp.bfloat16)
    slot_gate = jnp.sum(jnp.where(slot_hits, gate_weights[None, :, :], 0.0), axis=(1, 2))
    send_tokens = (
        jnp.dot(slot_token_b, tokens, preferred_element_type=jnp.float32)
        .astype(jnp.bfloat16)
        .reshape(owners, local_experts, capacity, model_width)
    )
    slot_target = jnp.dot(slot_token_b, cotangent, preferred_element_type=jnp.float32)
    send_slopes = (
        (slot_gate[:, None] * slot_target)
        .astype(jnp.bfloat16)
        .reshape(owners, local_experts, capacity, model_width)
    )
    gate_full, up_full, down_full = (
        lax.all_gather(gate_matrix, "dp", axis=0, tiled=True),
        lax.all_gather(up_matrix, "dp", axis=0, tiled=True),
        lax.all_gather(down_matrix, "dp", axis=0, tiled=True),
    )
    received = lax.all_to_all(send_tokens, "expert", split_axis=0, concat_axis=0, tiled=True)
    received, send_slopes = lax.optimization_barrier((received, send_slopes))
    slopes_in = lax.all_to_all(send_slopes, "expert", split_axis=0, concat_axis=0, tiled=True)
    pre_gate = jnp.einsum("sjcd,djf->sjcf", received, gate_full, preferred_element_type=jnp.float32)
    pre_up = jnp.einsum("sjcd,djf->sjcf", received, up_full, preferred_element_type=jnp.float32)
    expert_hidden = (jax.nn.silu(pre_gate) * pre_up).astype(jnp.bfloat16)
    outputs = jnp.einsum(
        "sjcf,djf->sjcd", expert_hidden, down_full, preferred_element_type=jnp.float32
    ).astype(jnp.bfloat16)
    hidden = expert_hidden
    outputs, slopes_in = lax.optimization_barrier((outputs, slopes_in))
    returned = lax.all_to_all(outputs, "expert", split_axis=0, concat_axis=0, tiled=True)
    hidden_slope = jnp.einsum(
        "sjcd,djf->sjcf", slopes_in, down_full, preferred_element_type=jnp.float32
    )
    sigmoid_gate = jax.nn.sigmoid(pre_gate)
    activation = pre_gate * sigmoid_gate
    expert_gate_slope = (
        hidden_slope * pre_up * sigmoid_gate * (1.0 + pre_gate * (1.0 - sigmoid_gate))
    ).astype(jnp.bfloat16)
    expert_up_slope = (hidden_slope * activation).astype(jnp.bfloat16)
    pick_slope = (
        jnp.einsum(
            "sjcf,djf->sjcd", expert_gate_slope, gate_full, preferred_element_type=jnp.float32
        )
        + jnp.einsum("sjcf,djf->sjcd", expert_up_slope, up_full, preferred_element_type=jnp.float32)
    ).astype(jnp.bfloat16)
    gate_slope, up_slope = (expert_gate_slope, expert_up_slope)
    pick_slope, returned = lax.optimization_barrier((pick_slope, returned))
    slopes_back = lax.all_to_all(pick_slope, "expert", split_axis=0, concat_axis=0, tiled=True)
    returned_rows = returned.reshape(slot_count, model_width)
    slot_mix = jnp.where(slot_token.T, slot_gate[None, :], 0.0)
    mix_high = slot_mix.astype(jnp.bfloat16)
    mix_low = (slot_mix - mix_high.astype(jnp.float32)).astype(jnp.bfloat16)
    mixed_out = (
        jnp.dot(mix_high, returned_rows, preferred_element_type=jnp.float32)
        + jnp.dot(mix_low, returned_rows, preferred_element_type=jnp.float32)
    ).astype(jnp.bfloat16)
    token_slot_slope = lax.dot_general(
        cotangent, returned_rows, (((1,), (1,)), ((), ())), preferred_element_type=jnp.float32
    )
    gate_slope_all = jnp.take_along_axis(token_slot_slope, position, axis=1)
    centred = gate_slope_all - jnp.sum(gate_weights * gate_slope_all, axis=1, keepdims=True)
    choice_slope = gate_weights * centred
    logit_slope = jnp.sum(onehot * choice_slope[:, :, None], axis=1)
    router_local = jnp.dot(tokens.astype(jnp.float32).T, logit_slope, precision=highest)
    devices_all = owners * lax.axis_size("dp")
    row_parts = router_local.reshape(devices_all, model_width // devices_all, experts_total)
    row_parts = lax.all_to_all(
        row_parts, ("dp", "expert"), split_axis=0, concat_axis=0, tiled=True
    )
    row_block = jnp.sum(row_parts, axis=0)
    row_copies = jnp.broadcast_to(row_block[None], (devices_all,) + row_block.shape)
    router_grad = lax.all_to_all(
        row_copies, ("dp", "expert"), split_axis=0, concat_axis=0, tiled=True
    ).reshape(model_width, experts_total)
    back_rows = slopes_back.reshape(slot_count, model_width)
    input_sum = lax.dot_general(
        slot_token_b, back_rows, (((0,), (0,)), ((), ())), preferred_element_type=jnp.float32
    )
    router_part = jnp.dot(logit_slope, router_weight.astype(jnp.float32).T, precision=highest)
    token_grad = (input_sum + router_part).astype(jnp.bfloat16)
    grad_gate_rows = jnp.einsum(
        "sjcd,sjcf->djf", received, gate_slope, preferred_element_type=jnp.float32
    )
    grad_up_rows = jnp.einsum(
        "sjcd,sjcf->djf", received, up_slope, preferred_element_type=jnp.float32
    )
    grad_down_rows = jnp.einsum(
        "sjcd,sjcf->djf", slopes_in, hidden, preferred_element_type=jnp.float32
    )
    summed = lax.psum_scatter(
        jnp.stack([grad_gate_rows, grad_up_rows, grad_down_rows], axis=1).astype(jnp.bfloat16),
        "dp",
        scatter_dimension=0,
        tiled=True,
    )
    gate_grad = summed[:, 0]
    up_grad = summed[:, 1]
    down_grad = summed[:, 2]
    return (mixed_out, token_grad, gate_grad, up_grad, down_grad, router_grad)


def solution(mesh):
    in_specs = (
        P(("dp", "expert"), None),
        P(),
        P(("dp", "expert"), None),
        P("dp", "expert", None),
        P("dp", "expert", None),
        P("dp", "expert", None),
        P(("dp", "expert"), None),
    )
    out_specs = (
        P(("dp", "expert"), None),
        P(("dp", "expert"), None),
        P("dp", "expert", None),
        P("dp", "expert", None),
        P("dp", "expert", None),
        P(),
    )
    return jax.shard_map(shards, mesh=mesh, in_specs=in_specs, out_specs=out_specs, check_vma=False)
```
